128 devices in a mesh: grid: 32 (over y, x, core), layer: 4 (over z).
Axes of the slice: x: 4, y: 4, z: 4, core: 2. Of those that a mesh axis runs over, the one named last changes fastest.
Arguments:
- h_blocks: bfloat16 [1024, 8, 128, 128], P('grid', 'layer'), may hold values from -0.09375 to 0.09375
- block_cols: int32 [1024, 8], P('grid', 'layer'), may hold values from 0 to 1023, as said below
- t_now: bfloat16 [131072, 1536], P(('grid', 'layer')), may hold values from -6 to 6
- t_prev: bfloat16 [131072, 1536], P(('grid', 'layer')), may hold values from -6 to 6
Outputs:
- next_term: bfloat16 [131072, 1536], P(('grid', 'layer'))
- after_term: bfloat16 [131072, 1536], P(('grid', 'layer'))
The draws below stay inside these ranges and needn't reach their ends.
Inputs may be any that keep to these rules, and one draw needn't show every extreme that they name: block_cols[i, 0] = i. With g = i // 32, every block column lies among the block rows g * 32 - 2 to g * 32 + 33 counted cyclically modulo 1024, and both ends of that range are named in every block row.
All inputs are finite; a program needn't handle non-finite values.
Results may differ from the reference program's by a relative error of at most 0.019.
Values may be sent and summed in bfloat16 or wider, within the bound.
No kernel may reach another device: no remote copies, remote signals or barrier semaphores. Data moves between devices by JAX's collectives and lax.ppermute only.
A program may use at most 192 MiB of HBM per device.

```python
import jax
import jax.numpy as jnp
from jax import lax

BS = 128
KB = 8
HB = 2
W = 1536
RB = 32
NB = 1024
N = 131072
N_LAYER = 4


def draw_block_cols(key, part):
    rows = jnp.arange(NB, dtype=jnp.int32)
    first = rows // RB * RB
    offsets = jax.random.randint(key, (NB, KB), -HB, RB + HB, dtype=jnp.int32)
    columns = (first[:, None] + offsets) % NB
    columns = columns.at[:, 0].set(rows)
    columns = columns.at[:, KB - 1].set((first + RB + HB - 1) % NB)
    columns = columns.at[:, KB - 2].set((first - HB + NB) % NB)
    return columns.astype(jnp.int32)


def levels(key, extent, cuts, low, largest):
    loudness, own = 1.0, jax.random.fold_in(key, 6)
    for dim, shards_of in cuts:
        heights = jnp.exp(jax.random.uniform(jax.random.fold_in(own, dim), (shards_of,), jnp.float32, low / len(cuts), largest / len(cuts)))
        loudness = loudness * jnp.repeat(heights, extent[dim] // shards_of).reshape([-1 if axis == dim else 1 for axis in range(len(extent))])
    return loudness


def centred(own_key, dims, deviation, most, cuts=(), kind=jnp.bfloat16):
    entries = jax.random.normal(own_key, dims, jnp.float32) * deviation
    if len(cuts) > 0:
        entries = levels(own_key, dims, cuts, -0.22, 0.18) * entries
    return jnp.clip(entries, min=-most, max=most).astype(kind)


def setup_inputs(seed: int = 0) -> dict:
    keys = jax.random.split(jax.random.key(seed), 5)
    return {
        "h_blocks": centred(keys[0], (NB, KB, BS, BS), (4 * KB * BS) ** -0.5, 0.09375, ((0, 32), (1, 4))),
        "block_cols": draw_block_cols(jax.random.fold_in(keys[4], 71), 0),
        "t_now": centred(keys[2], (N, W), 1.0, 6.0, ((0, 128),)),
        "t_prev": centred(keys[3], (N, W), 1.0, 6.0, ((0, 128),)),
    }


def apply_blocks(h_blocks, block_cols, field):
    panel = field.reshape(NB, BS, W)
    h_groups = h_blocks.reshape(NB // RB, RB, KB, BS, BS)
    c_groups = block_cols.reshape(NB // RB, RB, KB)

    def one_group(item):
        h_part, c_part = item
        picked = panel[c_part.astype(jnp.int32)].astype(jnp.float32)
        h_split = h_part.astype(jnp.float32).reshape(RB, N_LAYER, KB // N_LAYER, BS, BS)
        p_split = picked.reshape(RB, N_LAYER, KB // N_LAYER, BS, W)
        part = jnp.einsum('rqsij,rqsjc->qric', h_split, p_split)
        part = lax.optimization_barrier(part.astype(jnp.bfloat16)).astype(jnp.float32)
        return jnp.sum(part, axis=0)

    result = lax.map(one_group, (h_groups, c_groups))
    return result.reshape(NB * BS, W)


def reference(h_blocks, block_cols, t_now, t_prev):
    next_term = (2.0 * apply_blocks(h_blocks, block_cols, t_now) - t_prev.astype(jnp.float32)).astype(jnp.bfloat16)
    after_term = (2.0 * apply_blocks(h_blocks, block_cols, next_term) - t_now.astype(jnp.float32)).astype(jnp.bfloat16)
    return next_term, after_term
```

```python
import jax
import jax.numpy as jnp
from jax import lax
from jax.sharding import PartitionSpec as P

KB = 8
HB = 2
NCH = 4


def padded(array, width):
    size, length = (lax.axis_size("grid"), array.shape[0])
    up = [(i, (i + 1) % size) for i in range(size)]
    down = [(j, i) for i, j in up]
    before = lax.ppermute(array[length - width:], "grid", up)
    after = lax.ppermute(array[:width], "grid", down)
    return jnp.concatenate([before, array, after], axis=0)


def own_rows(h_own, rel_own, chunk):
    block_size = h_own.shape[2]
    panel = lax.all_gather(chunk, "layer", axis=0, tiled=True)
    wide = padded(panel, HB * block_size)
    blocks = wide.reshape(wide.shape[0] // block_size, block_size, chunk.shape[1])
    picked = blocks[rel_own]
    acc = jnp.einsum("rsij,rsjc->ric", h_own, picked, preferred_element_type=jnp.float32)
    return acc.reshape(chunk.shape[0], chunk.shape[1])


def shards(h_blocks, block_cols, t_now, t_prev):
    group_rows = h_blocks.shape[0]
    total_blocks = group_rows * lax.axis_size("grid")
    first_block = lax.axis_index("grid") * group_rows
    relative = (block_cols - first_block + HB + total_blocks) % total_blocks
    h_own = lax.all_to_all(h_blocks, "layer", 0, 1, tiled=True)
    rel_own = lax.all_to_all(relative, "layer", 0, 1, tiled=True)
    width = t_now.shape[1]
    step = width // NCH

    def recur(current, previous):
        outs = []
        for c in range(NCH):
            acc = own_rows(h_own, rel_own, current[c])
            outs.append((2.0 * acc - previous[c].astype(jnp.float32)).astype(jnp.bfloat16))
        return outs

    now_chunks = [t_now[:, c * step:(c + 1) * step] for c in range(NCH)]
    prev_chunks = [t_prev[:, c * step:(c + 1) * step] for c in range(NCH)]
    next_chunks = recur(now_chunks, prev_chunks)
    after_chunks = recur(next_chunks, now_chunks)
    return (jnp.concatenate(next_chunks, axis=1), jnp.concatenate(after_chunks, axis=1))


def solution(mesh):
    in_specs = (
        P("grid", "layer", None, None),
        P("grid", "layer"),
        P(("grid", "layer"), None),
        P(("grid", "layer"), None),
    )
    out_specs = (P(("grid", "layer"), None), P(("grid", "layer"), None))
    return jax.shard_map(shards, mesh=mesh, in_specs=in_specs, out_specs=out_specs, check_vma=False)
```

```python
import jax
import jax.numpy as jnp
from jax import lax
from jax.sharding import PartitionSpec as P

KB = 8
HB = 2
NCH = 2


def shift(size, k):
    return [(i, (i + k) % size) for i in range(size)]


def exchange(own, lidx, block_size):
    nl = lax.axis_size("layer")
    ng = lax.axis_size("grid")
    half = own.shape[0] // 2
    from_prev = lax.ppermute(own, "layer", shift(nl, 1))
    from_next = lax.ppermute(own, "layer", shift(nl, nl - 1))
    far_a = lax.ppermute(from_prev[:half], "layer", shift(nl, 1))
    far_b = lax.ppermute(from_next[half:], "layer", shift(nl, nl - 1))
    panel = jnp.concatenate([own, from_next, far_a, far_b, from_prev], axis=0)
    rows = own.shape[0]
    width = HB * block_size
    last_at = ((nl - 1 - lidx) % nl) * rows + rows - width
    first_at = ((0 - lidx) % nl) * rows
    last = lax.dynamic_slice_in_dim(panel, last_at, width, axis=0)
    first = lax.dynamic_slice_in_dim(panel, first_at, width, axis=0)
    lo = lax.ppermute(last, "grid", shift(ng, 1))
    hi = lax.ppermute(first, "grid", shift(ng, ng - 1))
    return jnp.concatenate([panel, lo, hi], axis=0)


def own_rows(h_own, pos_own, chunk, lidx):
    block_size = h_own.shape[2]
    wide = exchange(chunk, lidx, block_size)
    blocks = wide.reshape(wide.shape[0] // block_size, block_size, chunk.shape[1])
    picked = blocks[pos_own]
    acc = jnp.einsum("rsij,rsjc->ric", h_own, picked, preferred_element_type=jnp.float32)
    return acc.reshape(chunk.shape[0], chunk.shape[1])


def shards(h_blocks, block_cols, t_now, t_prev):
    group_rows, block_size = h_blocks.shape[0], h_blocks.shape[2]
    nl = lax.axis_size("layer")
    total_blocks = group_rows * lax.axis_size("grid")
    per_dev = group_rows // nl
    lidx = lax.axis_index("layer")
    first_block = lax.axis_index("grid") * group_rows
    rel = (block_cols - first_block + HB + total_blocks) % total_blocks

    h_split = h_blocks.reshape(nl, per_dev, *h_blocks.shape[1:])
    p_split = rel.reshape(nl, per_dev, rel.shape[1])
    h_parts = [lax.dynamic_index_in_dim(h_split, lidx, 0, keepdims=False)]
    p_parts = [lax.dynamic_index_in_dim(p_split, lidx, 0, keepdims=False)]
    for k in range(1, nl):
        dest = (lidx + k) % nl
        h_parts.append(lax.ppermute(lax.dynamic_index_in_dim(h_split, dest, 0, keepdims=False), "layer", shift(nl, k)))
        p_parts.append(lax.ppermute(lax.dynamic_index_in_dim(p_split, dest, 0, keepdims=False), "layer", shift(nl, k)))
    h_own = jnp.concatenate(h_parts, axis=1)
    rel_own = jnp.concatenate(p_parts, axis=1)
    inner = rel_own - HB
    owner = inner // per_dev
    pos_own = ((owner - lidx) % nl) * per_dev + inner % per_dev
    pos_own = jnp.where(rel_own < HB, nl * per_dev + rel_own, pos_own)
    pos_own = jnp.where(rel_own >= HB + group_rows, rel_own, pos_own)

    width = t_now.shape[1]
    step = width // NCH

    def recur(current, previous):
        outs = []
        for c in range(NCH):
            acc = own_rows(h_own, pos_own, current[c], lidx)
            outs.append((2.0 * acc - previous[c].astype(jnp.float32)).astype(jnp.bfloat16))
        return outs

    now_chunks = [t_now[:, c * step:(c + 1) * step] for c in range(NCH)]
    prev_chunks = [t_prev[:, c * step:(c + 1) * step] for c in range(NCH)]
    next_chunks = recur(now_chunks, prev_chunks)
    after_chunks = recur(next_chunks, now_chunks)
    return (jnp.concatenate(next_chunks, axis=1), jnp.concatenate(after_chunks, axis=1))


def solution(mesh):
    in_specs = (
        P("grid", "layer", None, None),
        P("grid", "layer"),
        P(("grid", "layer"), None),
        P(("grid", "layer"), None),
    )
    out_specs = (P(("grid", "layer"), None), P(("grid", "layer"), None))
    return jax.shard_map(shards, mesh=mesh, in_specs=in_specs, out_specs=out_specs, check_vma=False)
```

```python
import jax
import jax.numpy as jnp
from jax import lax
from jax.sharding import PartitionSpec as P
from jax.experimental import pallas as pl
from jax.experimental.pallas import tpu as pltpu

KB = 8
HB = 2
NCH = 2


def shift(size, k):
    return [(i, (i + k) % size) for i in range(size)]


def exchange(own, lidx, block_size):
    nl = lax.axis_size("layer")
    ng = lax.axis_size("grid")
    half = own.shape[0] // 2
    from_prev = lax.ppermute(own, "layer", shift(nl, 1))
    from_next = lax.ppermute(own, "layer", shift(nl, nl - 1))
    far_a = lax.ppermute(from_prev[:half], "layer", shift(nl, 1))
    far_b = lax.ppermute(from_next[half:], "layer", shift(nl, nl - 1))
    panel = jnp.concatenate([own, from_next, far_a, far_b, from_prev], axis=0)
    rows = own.shape[0]
    width = HB * block_size
    last_at = ((nl - 1 - lidx) % nl) * rows + rows - width
    first_at = ((0 - lidx) % nl) * rows
    last = lax.dynamic_slice_in_dim(panel, last_at, width, axis=0)
    first = lax.dynamic_slice_in_dim(panel, first_at, width, axis=0)
    lo = lax.ppermute(last, "grid", shift(ng, 1))
    hi = lax.ppermute(first, "grid", shift(ng, ng - 1))
    return jnp.concatenate([panel, lo, hi], axis=0)


def step_kernel(pos_ref, h_ref, *refs):
    slots = h_ref.shape[1]
    panel_refs, prev_ref, out_ref = refs[:slots], refs[slots], refs[slots + 1]
    acc = jnp.dot(h_ref[0, 0], panel_refs[0][0], preferred_element_type=jnp.float32)
    for s in range(1, slots):
        acc = acc + jnp.dot(h_ref[0, s], panel_refs[s][0], preferred_element_type=jnp.float32)
    out_ref[...] = (2.0 * acc - prev_ref[...].astype(jnp.float32)).astype(out_ref.dtype)


def own_rows(h_own, pos_flat, chunk, previous, lidx):
    rows, slots, block_size = h_own.shape[0], h_own.shape[1], h_own.shape[2]
    width = chunk.shape[1]
    wide = exchange(chunk, lidx, block_size)
    blocks = wide.reshape(wide.shape[0] // block_size, block_size, width)

    def panel_map(s):
        return lambda i, p: (p[i * slots + s], 0, 0)

    in_specs = [pl.BlockSpec((1, slots, block_size, block_size), lambda i, p: (i, 0, 0, 0))]
    in_specs += [pl.BlockSpec((1, block_size, width), panel_map(s)) for s in range(slots)]
    in_specs += [pl.BlockSpec((block_size, width), lambda i, p: (i, 0))]
    grid_spec = pltpu.PrefetchScalarGridSpec(
        num_scalar_prefetch=1,
        grid=(rows,),
        in_specs=in_specs,
        out_specs=pl.BlockSpec((block_size, width), lambda i, p: (i, 0)),
    )
    return pl.pallas_call(
        step_kernel,
        grid_spec=grid_spec,
        out_shape=jax.ShapeDtypeStruct(chunk.shape, jnp.bfloat16),
    )(pos_flat, h_own, *([blocks] * slots), previous)


def shards(h_blocks, block_cols, t_now, t_prev):
    group_rows, block_size = h_blocks.shape[0], h_blocks.shape[2]
    nl = lax.axis_size("layer")
    total_blocks = group_rows * lax.axis_size("grid")
    per_dev = group_rows // nl
    lidx = lax.axis_index("layer")
    first_block = lax.axis_index("grid") * group_rows
    rel = (block_cols - first_block + HB + total_blocks) % total_blocks

    h_split = h_blocks.reshape(nl, per_dev, *h_blocks.shape[1:])
    p_split = rel.reshape(nl, per_dev, rel.shape[1])
    h_parts = [lax.dynamic_index_in_dim(h_split, lidx, 0, keepdims=False)]
    p_parts = [lax.dynamic_index_in_dim(p_split, lidx, 0, keepdims=False)]
    for k in range(1, nl):
        dest = (lidx + k) % nl
        h_parts.append(lax.ppermute(lax.dynamic_index_in_dim(h_split, dest, 0, keepdims=False), "layer", shift(nl, k)))
        p_parts.append(lax.ppermute(lax.dynamic_index_in_dim(p_split, dest, 0, keepdims=False), "layer", shift(nl, k)))
    h_own = jnp.concatenate(h_parts, axis=1)
    rel_own = jnp.concatenate(p_parts, axis=1)
    inner = rel_own - HB
    owner = inner // per_dev
    pos_own = ((owner - lidx) % nl) * per_dev + inner % per_dev
    pos_own = jnp.where(rel_own < HB, nl * per_dev + rel_own, pos_own)
    pos_own = jnp.where(rel_own >= HB + group_rows, rel_own, pos_own)

    pos_flat = pos_own.reshape(-1).astype(jnp.int32)
    width = t_now.shape[1]
    step = width // NCH

    def recur(current, previous):
        outs = []
        for c in range(NCH):
            outs.append(own_rows(h_own, pos_flat, current[c], previous[c], lidx))
        return outs

    now_chunks = [t_now[:, c * step:(c + 1) * step] for c in range(NCH)]
    prev_chunks = [t_prev[:, c * step:(c + 1) * step] for c in range(NCH)]
    next_chunks = recur(now_chunks, prev_chunks)
    after_chunks = recur(next_chunks, now_chunks)
    return (jnp.concatenate(next_chunks, axis=1), jnp.concatenate(after_chunks, axis=1))


def solution(mesh):
    in_specs = (
        P("grid", "layer", None, None),
        P("grid", "layer"),
        P(("grid", "layer"), None),
        P(("grid", "layer"), None),
    )
    out_specs = (P(("grid", "layer"), None), P(("grid", "layer"), None))
    return jax.shard_map(shards, mesh=mesh, in_specs=in_specs, out_specs=out_specs, check_vma=False)
```

```python
import functools

import jax
import jax.numpy as jnp
from jax import lax
from jax.sharding import PartitionSpec as P
from jax.experimental import pallas as pl
from jax.experimental.pallas import tpu as pltpu

KB = 8
HB = 2
NCH = 2
TILE = 256


def shift(size, k):
    return [(i, (i + k) % size) for i in range(size)]


def exchange(own, lidx, block_size):
    nl = lax.axis_size("layer")
    ng = lax.axis_size("grid")
    half = own.shape[0] // 2
    width = HB * block_size
    from_prev = lax.ppermute(own, "layer", shift(nl, 1))
    from_next = lax.ppermute(own, "layer", shift(nl, nl - 1))
    far_a = lax.ppermute(from_prev[:half], "layer", shift(nl, 1))
    far_b = lax.ppermute(from_next[half:], "layer", shift(nl, nl - 1))
    tails = jnp.concatenate([a[-width:] for a in (own, from_next, far_b, from_prev)], axis=0)
    heads = jnp.concatenate([a[:width] for a in (own, from_next, far_a, from_prev)], axis=0)
    last = lax.dynamic_slice_in_dim(tails, ((nl - 1 - lidx) % nl) * width, width, axis=0)
    first = lax.dynamic_slice_in_dim(heads, ((0 - lidx) % nl) * width, width, axis=0)
    lo = lax.ppermute(last, "grid", shift(ng, 1))
    hi = lax.ppermute(first, "grid", shift(ng, ng - 1))
    return [own, from_next, far_a, far_b, from_prev, lo, hi]


def step_kernel(pos_ref, h_ref, *refs, starts, tile_rows):
    n_pieces = len(starts) - 1
    pieces, prev_ref, out_ref, acc_ref = refs[:n_pieces], refs[n_pieces], refs[n_pieces + 1], refs[n_pieces + 2]
    rows, slots = h_ref.shape[0], h_ref.shape[1]

    def row(i, carry):
        acc_ref[...] = jnp.zeros_like(acc_ref)
        for s in range(slots):
            p = pos_ref[i * slots + s]
            for k in range(n_pieces):
                lo, hi = starts[k], starts[k + 1]

                @pl.when((p >= lo) & (p < hi))
                def _():
                    acc_ref[...] += jnp.dot(h_ref[i, s], pieces[k][p - lo], preferred_element_type=jnp.float32)

        at = pl.multiple_of(i * tile_rows, tile_rows)
        prev = prev_ref[pl.ds(at, tile_rows), :].astype(jnp.float32)
        out_ref[pl.ds(at, tile_rows), :] = (2.0 * acc_ref[...] - prev).astype(out_ref.dtype)
        return carry

    lax.fori_loop(0, rows, row, 0)


def own_rows(h_own, pos_flat, chunk, previous, lidx):
    rows, slots, block_size = h_own.shape[0], h_own.shape[1], h_own.shape[2]
    width = chunk.shape[1]
    tile = TILE if width % TILE == 0 else width
    pieces = [a.reshape(a.shape[0] // block_size, block_size, width) for a in exchange(chunk, lidx, block_size)]
    starts = [0]
    for a in pieces:
        starts.append(starts[-1] + a.shape[0])
    in_specs = [pl.BlockSpec(h_own.shape, lambda j, p: (0, 0, 0, 0))]
    in_specs += [pl.BlockSpec((a.shape[0], block_size, tile), lambda j, p: (0, 0, j)) for a in pieces]
    in_specs += [pl.BlockSpec((chunk.shape[0], tile), lambda j, p: (0, j))]
    grid_spec = pltpu.PrefetchScalarGridSpec(
        num_scalar_prefetch=1,
        grid=(width // tile,),
        in_specs=in_specs,
        out_specs=pl.BlockSpec((chunk.shape[0], tile), lambda j, p: (0, j)),
        scratch_shapes=[pltpu.VMEM((block_size, tile), jnp.float32)],
    )
    kernel = functools.partial(step_kernel, starts=tuple(starts), tile_rows=block_size)
    return pl.pallas_call(
        kernel,
        grid_spec=grid_spec,
        out_shape=jax.ShapeDtypeStruct(chunk.shape, jnp.bfloat16),
    )(pos_flat, h_own, *pieces, previous)


def shards(h_blocks, block_cols, t_now, t_prev):
    group_rows, block_size = h_blocks.shape[0], h_blocks.shape[2]
    nl = lax.axis_size("layer")
    total_blocks = group_rows * lax.axis_size("grid")
    per_dev = group_rows // nl
    lidx = lax.axis_index("layer")
    first_block = lax.axis_index("grid") * group_rows
    rel = (block_cols - first_block + HB + total_blocks) % total_blocks

    h_split = h_blocks.reshape(nl, per_dev, *h_blocks.shape[1:])
    p_split = rel.reshape(nl, per_dev, rel.shape[1])
    h_parts = [lax.dynamic_index_in_dim(h_split, lidx, 0, keepdims=False)]
    p_parts = [lax.dynamic_index_in_dim(p_split, lidx, 0, keepdims=False)]
    for k in range(1, nl):
        dest = (lidx + k) % nl
        h_parts.append(lax.ppermute(lax.dynamic_index_in_dim(h_split, dest, 0, keepdims=False), "layer", shift(nl, k)))
        p_parts.append(lax.ppermute(lax.dynamic_index_in_dim(p_split, dest, 0, keepdims=False), "layer", shift(nl, k)))
    h_own = jnp.concatenate(h_parts, axis=1)
    rel_own = jnp.concatenate(p_parts, axis=1)
    inner = rel_own - HB
    owner = inner // per_dev
    pos_own = ((owner - lidx) % nl) * per_dev + inner % per_dev
    pos_own = jnp.where(rel_own < HB, nl * per_dev + rel_own, pos_own)
    pos_own = jnp.where(rel_own >= HB + group_rows, rel_own, pos_own)

    pos_flat = pos_own.reshape(-1).astype(jnp.int32)
    width = t_now.shape[1]
    step = width // NCH

    def recur(current, previous):
        outs = []
        for c in range(NCH):
            outs.append(own_rows(h_own, pos_flat, current[c], previous[c], lidx))
        return outs

    now_chunks = [t_now[:, c * step:(c + 1) * step] for c in range(NCH)]
    prev_chunks = [t_prev[:, c * step:(c + 1) * step] for c in range(NCH)]
    next_chunks = recur(now_chunks, prev_chunks)
    after_chunks = recur(next_chunks, now_chunks)
    return (jnp.concatenate(next_chunks, axis=1), jnp.concatenate(after_chunks, axis=1))


def solution(mesh):
    in_specs = (
        P("grid", "layer", None, None),
        P("grid", "layer"),
        P(("grid", "layer"), None),
        P(("grid", "layer"), None),
    )
    out_specs = (P(("grid", "layer"), None), P(("grid", "layer"), None))
    return jax.shard_map(shards, mesh=mesh, in_specs=in_specs, out_specs=out_specs, check_vma=False)
```

```python
import jax
import jax.numpy as jnp
from jax import lax
from jax.sharding import PartitionSpec as P
from jax.experimental import pallas as pl
from jax.experimental.pallas import tpu as pltpu

KB = 8
HB = 2
NCH = 1


def shift(size, k):
    return [(i, (i + k) % size) for i in range(size)]


def exchange(own, lidx, block_size):
    nl = lax.axis_size("layer")
    ng = lax.axis_size("grid")
    half = own.shape[0] // 2
    from_prev = lax.ppermute(own, "layer", shift(nl, 1))
    from_next = lax.ppermute(own, "layer", shift(nl, nl - 1))
    far_a = lax.ppermute(from_prev[:half], "layer", shift(nl, 1))
    far_b = lax.ppermute(from_next[half:], "layer", shift(nl, nl - 1))
    panel = jnp.concatenate([own, from_next, far_a, far_b, from_prev], axis=0)
    rows = own.shape[0]
    width = HB * block_size
    last_at = ((nl - 1 - lidx) % nl) * rows + rows - width
    first_at = ((0 - lidx) % nl) * rows
    last = lax.dynamic_slice_in_dim(panel, last_at, width, axis=0)
    first = lax.dynamic_slice_in_dim(panel, first_at, width, axis=0)
    lo = lax.ppermute(last, "grid", shift(ng, 1))
    hi = lax.ppermute(first, "grid", shift(ng, ng - 1))
    return jnp.concatenate([panel, lo, hi], axis=0)


def step_kernel(pos_ref, h_ref, *refs):
    slots = h_ref.shape[1]
    panel_refs, prev_ref, out_ref = refs[:slots], refs[slots], refs[slots + 1]
    acc = jnp.dot(h_ref[0, 0], panel_refs[0][0], preferred_element_type=jnp.float32)
    for s in range(1, slots):
        acc = acc + jnp.dot(h_ref[0, s], panel_refs[s][0], preferred_element_type=jnp.float32)
    out_ref[...] = (2.0 * acc - prev_ref[...].astype(jnp.float32)).astype(out_ref.dtype)


def own_rows(h_own, pos_flat, chunk, previous, lidx):
    rows, slots, block_size = h_own.shape[0], h_own.shape[1], h_own.shape[2]
    width = chunk.shape[1]
    wide = exchange(chunk, lidx, block_size)
    blocks = wide.reshape(wide.shape[0] // block_size, block_size, width)

    def panel_map(s):
        return lambda i, p: (p[i * slots + s], 0, 0)

    in_specs = [pl.BlockSpec((1, slots, block_size, block_size), lambda i, p: (i, 0, 0, 0))]
    in_specs += [pl.BlockSpec((1, block_size, width), panel_map(s)) for s in range(slots)]
    in_specs += [pl.BlockSpec((block_size, width), lambda i, p: (i, 0))]
    grid_spec = pltpu.PrefetchScalarGridSpec(
        num_scalar_prefetch=1,
        grid=(rows,),
        in_specs=in_specs,
        out_specs=pl.BlockSpec((block_size, width), lambda i, p: (i, 0)),
    )
    return pl.pallas_call(
        step_kernel,
        grid_spec=grid_spec,
        out_shape=jax.ShapeDtypeStruct(chunk.shape, jnp.bfloat16),
    )(pos_flat, h_own, *([blocks] * slots), previous)


def shards(h_blocks, block_cols, t_now, t_prev):
    group_rows, block_size = h_blocks.shape[0], h_blocks.shape[2]
    nl = lax.axis_size("layer")
    total_blocks = group_rows * lax.axis_size("grid")
    per_dev = group_rows // nl
    lidx = lax.axis_index("layer")
    first_block = lax.axis_index("grid") * group_rows
    rel = (block_cols - first_block + HB + total_blocks) % total_blocks

    h_split = h_blocks.reshape(nl, per_dev, *h_blocks.shape[1:])
    p_split = rel.reshape(nl, per_dev, rel.shape[1])
    h_parts = [lax.dynamic_index_in_dim(h_split, lidx, 0, keepdims=False)]
    p_parts = [lax.dynamic_index_in_dim(p_split, lidx, 0, keepdims=False)]
    for k in range(1, nl):
        dest = (lidx + k) % nl
        h_parts.append(lax.ppermute(lax.dynamic_index_in_dim(h_split, dest, 0, keepdims=False), "layer", shift(nl, k)))
        p_parts.append(lax.ppermute(lax.dynamic_index_in_dim(p_split, dest, 0, keepdims=False), "layer", shift(nl, k)))
    h_own = jnp.concatenate(h_parts, axis=1)
    rel_own = jnp.concatenate(p_parts, axis=1)
    inner = rel_own - HB
    owner = inner // per_dev
    pos_own = ((owner - lidx) % nl) * per_dev + inner % per_dev
    pos_own = jnp.where(rel_own < HB, nl * per_dev + rel_own, pos_own)
    pos_own = jnp.where(rel_own >= HB + group_rows, rel_own, pos_own)

    pos_flat = pos_own.reshape(-1).astype(jnp.int32)
    width = t_now.shape[1]
    step = width // NCH

    def recur(current, previous):
        outs = []
        for c in range(NCH):
            outs.append(own_rows(h_own, pos_flat, current[c], previous[c], lidx))
        return outs

    now_chunks = [t_now[:, c * step:(c + 1) * step] for c in range(NCH)]
    prev_chunks = [t_prev[:, c * step:(c + 1) * step] for c in range(NCH)]
    next_chunks = recur(now_chunks, prev_chunks)
    after_chunks = recur(next_chunks, now_chunks)
    return (jnp.concatenate(next_chunks, axis=1), jnp.concatenate(after_chunks, axis=1))


def solution(mesh):
    in_specs = (
        P("grid", "layer", None, None),
        P("grid", "layer"),
        P(("grid", "layer"), None),
        P(("grid", "layer"), None),
    )
    out_specs = (P(("grid", "layer"), None), P(("grid", "layer"), None))
    return jax.shard_map(shards, mesh=mesh, in_specs=in_specs, out_specs=out_specs, check_vma=False)
```

```python
import jax
import jax.numpy as jnp
from jax import lax
from jax.sharding import PartitionSpec as P
from jax.experimental import pallas as pl
from jax.experimental.pallas import tpu as pltpu

KB = 8
HB = 2
NCH = 1


def shift(size, k):
    return [(i, (i + k) % size) for i in range(size)]


def exchange(own, lidx, block_size):
    nl = lax.axis_size("layer")
    ng = lax.axis_size("grid")
    half = own.shape[0] // 2
    width = HB * block_size
    from_prev = lax.ppermute(own, "layer", shift(nl, 1))
    from_next = lax.ppermute(own, "layer", shift(nl, nl - 1))
    far_a = lax.ppermute(from_prev[:half], "layer", shift(nl, 1))
    far_b = lax.ppermute(from_next[half:], "layer", shift(nl, nl - 1))
    tails = jnp.concatenate([a[-width:] for a in (own, from_next, far_b, from_prev)], axis=0)
    heads = jnp.concatenate([a[:width] for a in (own, from_next, far_a, from_prev)], axis=0)
    last = lax.dynamic_slice_in_dim(tails, ((nl - 1 - lidx) % nl) * width, width, axis=0)
    first = lax.dynamic_slice_in_dim(heads, ((0 - lidx) % nl) * width, width, axis=0)
    lo = lax.ppermute(last, "grid", shift(ng, 1))
    hi = lax.ppermute(first, "grid", shift(ng, ng - 1))
    near = jnp.concatenate([own, from_next, from_prev], axis=0)
    far = jnp.concatenate([far_a, far_b, lo, hi], axis=0)
    return near, far


def near_kernel(pos_ref, h_ref, *refs):
    slots = h_ref.shape[1]
    panel_refs, out_ref = refs[:slots], refs[slots]
    acc = jnp.dot(h_ref[0, 0], panel_refs[0][0], preferred_element_type=jnp.float32)
    for s in range(1, slots):
        acc = acc + jnp.dot(h_ref[0, s], panel_refs[s][0], preferred_element_type=jnp.float32)
    out_ref[...] = acc


def far_kernel(pos_ref, h_ref, *refs):
    slots = h_ref.shape[1]
    panel_refs, acc_ref, prev_ref, out_ref = refs[:slots], refs[slots], refs[slots + 1], refs[slots + 2]
    acc = acc_ref[...]
    for s in range(slots):
        acc = acc + jnp.dot(h_ref[0, s], panel_refs[s][0], preferred_element_type=jnp.float32)
    out_ref[...] = (2.0 * acc - prev_ref[...].astype(jnp.float32)).astype(out_ref.dtype)


def picked_call(kernel, pos_flat, h_part, blocks, extra, out_dtype):
    rows, slots, block_size = h_part.shape[0], h_part.shape[1], h_part.shape[2]
    width = blocks.shape[2]

    def panel_map(s):
        return lambda i, p: (p[i * slots + s], 0, 0)

    in_specs = [pl.BlockSpec((1, slots, block_size, block_size), lambda i, p: (i, 0, 0, 0))]
    in_specs += [pl.BlockSpec((1, block_size, width), panel_map(s)) for s in range(slots)]
    in_specs += [pl.BlockSpec((block_size, width), lambda i, p: (i, 0)) for _ in extra]
    grid_spec = pltpu.PrefetchScalarGridSpec(
        num_scalar_prefetch=1,
        grid=(rows,),
        in_specs=in_specs,
        out_specs=pl.BlockSpec((block_size, width), lambda i, p: (i, 0)),
    )
    return pl.pallas_call(
        kernel,
        grid_spec=grid_spec,
        out_shape=jax.ShapeDtypeStruct((rows * block_size, width), out_dtype),
    )(pos_flat, h_part, *([blocks] * slots), *extra)


def own_rows(parts, chunk, previous, lidx):
    (h_near, near_pos), (h_far, far_pos) = parts
    block_size = h_near.shape[2]
    width = chunk.shape[1]
    near, far = exchange(chunk, lidx, block_size)
    near = near.reshape(near.shape[0] // block_size, block_size, width)
    far = far.reshape(far.shape[0] // block_size, block_size, width)
    acc = picked_call(near_kernel, near_pos, h_near, near, [], jnp.float32)
    return picked_call(far_kernel, far_pos, h_far, far, [acc, previous], jnp.bfloat16)


def carried(valid, pos):
    out, last = [], jnp.zeros_like(pos[0])
    for i in range(pos.shape[0]):
        last = jnp.where(valid[i], pos[i], last)
        out.append(last)
    return jnp.stack(out).reshape(-1).astype(jnp.int32)


def shards(h_blocks, block_cols, t_now, t_prev):
    group_rows, block_size = h_blocks.shape[0], h_blocks.shape[2]
    nl = lax.axis_size("layer")
    total_blocks = group_rows * lax.axis_size("grid")
    per_dev = group_rows // nl
    lidx = lax.axis_index("layer")
    first_block = lax.axis_index("grid") * group_rows
    rel = (block_cols - first_block + HB + total_blocks) % total_blocks

    h_split = h_blocks.reshape(nl, per_dev, *h_blocks.shape[1:])
    p_split = rel.reshape(nl, per_dev, rel.shape[1])
    h_parts = [lax.dynamic_index_in_dim(h_split, lidx, 0, keepdims=False)]
    p_parts = [lax.dynamic_index_in_dim(p_split, lidx, 0, keepdims=False)]
    for k in range(1, nl):
        dest = (lidx + k) % nl
        h_parts.append(lax.ppermute(lax.dynamic_index_in_dim(h_split, dest, 0, keepdims=False), "layer", shift(nl, k)))
        p_parts.append(lax.ppermute(lax.dynamic_index_in_dim(p_split, dest, 0, keepdims=False), "layer", shift(nl, k)))
    h_own = jnp.concatenate(h_parts, axis=1)
    rel_own = jnp.concatenate(p_parts, axis=1)
    inner = rel_own - HB
    owner = inner // per_dev
    pos_own = ((owner - lidx) % nl) * per_dev + inner % per_dev
    pos_own = jnp.where(rel_own < HB, nl * per_dev + rel_own, pos_own)
    pos_own = jnp.where(rel_own >= HB + group_rows, rel_own, pos_own)

    is_near = (pos_own < 2 * per_dev) | ((pos_own >= 3 * per_dev) & (pos_own < nl * per_dev))
    near_pos = jnp.where(pos_own < 2 * per_dev, pos_own, pos_own - per_dev)
    near_pos = jnp.where(is_near, near_pos, 0)
    far_pos = jnp.where(pos_own >= nl * per_dev, pos_own - 3 * per_dev, pos_own - 2 * per_dev)
    far_pos = jnp.where(is_near, 0, far_pos)
    zero = jnp.zeros((), h_own.dtype)
    parts = (
        (jnp.where(is_near[:, :, None, None], h_own, zero), carried(is_near, near_pos)),
        (jnp.where(is_near[:, :, None, None], zero, h_own), carried(~is_near, far_pos)),
    )
    width = t_now.shape[1]
    step = width // NCH

    def recur(current, previous):
        outs = []
        for c in range(NCH):
            outs.append(own_rows(parts, current[c], previous[c], lidx))
        return outs

    now_chunks = [t_now[:, c * step:(c + 1) * step] for c in range(NCH)]
    prev_chunks = [t_prev[:, c * step:(c + 1) * step] for c in range(NCH)]
    next_chunks = recur(now_chunks, prev_chunks)
    after_chunks = recur(next_chunks, now_chunks)
    return (jnp.concatenate(next_chunks, axis=1), jnp.concatenate(after_chunks, axis=1))


def solution(mesh):
    in_specs = (
        P("grid", "layer", None, None),
        P("grid", "layer"),
        P(("grid", "layer"), None),
        P(("grid", "layer"), None),
    )
    out_specs = (P(("grid", "layer"), None), P(("grid", "layer"), None))
    return jax.shard_map(shards, mesh=mesh, in_specs=in_specs, out_specs=out_specs, check_vma=False)
```

```python
import jax
import jax.numpy as jnp
from jax import lax
from jax.sharding import PartitionSpec as P
from jax.experimental import pallas as pl
from jax.experimental.pallas import tpu as pltpu

KB = 8
HB = 2
NCH = 2


def shift(size, k):
    return [(i, (i + k) % size) for i in range(size)]


def exchange(own, lidx, block_size):
    nl = lax.axis_size("layer")
    ng = lax.axis_size("grid")
    half = own.shape[0] // 2
    width = HB * block_size
    from_prev = lax.ppermute(own, "layer", shift(nl, 1))
    from_next = lax.ppermute(own, "layer", shift(nl, nl - 1))
    far_a = lax.ppermute(from_prev[:half], "layer", shift(nl, 1))
    far_b = lax.ppermute(from_next[half:], "layer", shift(nl, nl - 1))
    tails = jnp.concatenate([a[-width:] for a in (own, from_next, far_b, from_prev)], axis=0)
    heads = jnp.concatenate([a[:width] for a in (own, from_next, far_a, from_prev)], axis=0)
    last = lax.dynamic_slice_in_dim(tails, ((nl - 1 - lidx) % nl) * width, width, axis=0)
    first = lax.dynamic_slice_in_dim(heads, ((0 - lidx) % nl) * width, width, axis=0)
    lo = lax.ppermute(last, "grid", shift(ng, 1))
    hi = lax.ppermute(first, "grid", shift(ng, ng - 1))
    return jnp.concatenate([own, from_next, far_a, far_b, from_prev, lo, hi], axis=0)


def step_kernel(pos_ref, h_ref, *refs):
    slots = h_ref.shape[1]
    panel_refs, prev_ref, out_ref = refs[:slots], refs[slots], refs[slots + 1]
    acc = jnp.dot(h_ref[0, 0], panel_refs[0][0], preferred_element_type=jnp.float32)
    for s in range(1, slots):
        acc = acc + jnp.dot(h_ref[0, s], panel_refs[s][0], preferred_element_type=jnp.float32)
    out_ref[...] = (2.0 * acc - prev_ref[...].astype(jnp.float32)).astype(out_ref.dtype)


def own_rows(h_own, pos_flat, chunk, previous, lidx):
    rows, slots, block_size = h_own.shape[0], h_own.shape[1], h_own.shape[2]
    width = chunk.shape[1]
    wide = exchange(chunk, lidx, block_size)
    blocks = wide.reshape(wide.shape[0] // block_size, block_size, width)

    def panel_map(s):
        return lambda i, p: (p[i * slots + s], 0, 0)

    in_specs = [pl.BlockSpec((1, slots, block_size, block_size), lambda i, p: (i, 0, 0, 0))]
    in_specs += [pl.BlockSpec((1, block_size, width), panel_map(s)) for s in range(slots)]
    in_specs += [pl.BlockSpec((block_size, width), lambda i, p: (i, 0))]
    grid_spec = pltpu.PrefetchScalarGridSpec(
        num_scalar_prefetch=1,
        grid=(rows,),
        in_specs=in_specs,
        out_specs=pl.BlockSpec((block_size, width), lambda i, p: (i, 0)),
    )
    return pl.pallas_call(
        step_kernel,
        grid_spec=grid_spec,
        out_shape=jax.ShapeDtypeStruct(chunk.shape, jnp.bfloat16),
    )(pos_flat, h_own, *([blocks] * slots), previous)


def shards(h_blocks, block_cols, t_now, t_prev):
    group_rows, block_size = h_blocks.shape[0], h_blocks.shape[2]
    nl = lax.axis_size("layer")
    total_blocks = group_rows * lax.axis_size("grid")
    per_dev = group_rows // nl
    lidx = lax.axis_index("layer")
    first_block = lax.axis_index("grid") * group_rows
    rel = (block_cols - first_block + HB + total_blocks) % total_blocks

    h_split = h_blocks.reshape(nl, per_dev, *h_blocks.shape[1:])
    p_split = rel.reshape(nl, per_dev, rel.shape[1])
    h_parts = [lax.dynamic_index_in_dim(h_split, lidx, 0, keepdims=False)]
    p_parts = [lax.dynamic_index_in_dim(p_split, lidx, 0, keepdims=False)]
    for k in range(1, nl):
        dest = (lidx + k) % nl
        h_parts.append(lax.ppermute(lax.dynamic_index_in_dim(h_split, dest, 0, keepdims=False), "layer", shift(nl, k)))
        p_parts.append(lax.ppermute(lax.dynamic_index_in_dim(p_split, dest, 0, keepdims=False), "layer", shift(nl, k)))
    h_own = jnp.concatenate(h_parts, axis=1)
    rel_own = jnp.concatenate(p_parts, axis=1)
    inner = rel_own - HB
    owner = inner // per_dev
    pos_own = ((owner - lidx) % nl) * per_dev + inner % per_dev
    pos_own = jnp.where(rel_own < HB, nl * per_dev + rel_own, pos_own)
    pos_own = jnp.where(rel_own >= HB + group_rows, rel_own, pos_own)

    pos_flat = pos_own.reshape(-1).astype(jnp.int32)
    width = t_now.shape[1]
    step = width // NCH

    def recur(current, previous):
        outs = []
        for c in range(NCH):
            outs.append(own_rows(h_own, pos_flat, current[c], previous[c], lidx))
        return outs

    now_chunks = [t_now[:, c * step:(c + 1) * step] for c in range(NCH)]
    prev_chunks = [t_prev[:, c * step:(c + 1) * step] for c in range(NCH)]
    next_chunks = recur(now_chunks, prev_chunks)
    after_chunks = recur(next_chunks, now_chunks)
    return (jnp.concatenate(next_chunks, axis=1), jnp.concatenate(after_chunks, axis=1))


def solution(mesh):
    in_specs = (
        P("grid", "layer", None, None),
        P("grid", "layer"),
        P(("grid", "layer"), None),
        P(("grid", "layer"), None),
    )
    out_specs = (P(("grid", "layer"), None), P(("grid", "layer"), None))
    return jax.shard_map(shards, mesh=mesh, in_specs=in_specs, out_specs=out_specs, check_vma=False)
```

```python
import jax
import jax.numpy as jnp
from jax import lax
from jax.sharding import PartitionSpec as P
from jax.experimental import pallas as pl
from jax.experimental.pallas import tpu as pltpu

KB = 8
HB = 2
NCH = 2
TILE = 384


def shift(size, k):
    return [(i, (i + k) % size) for i in range(size)]


def exchange(own, lidx, block_size):
    nl = lax.axis_size("layer")
    ng = lax.axis_size("grid")
    half = own.shape[0] // 2
    from_prev = lax.ppermute(own, "layer", shift(nl, 1))
    from_next = lax.ppermute(own, "layer", shift(nl, nl - 1))
    far_a = lax.ppermute(from_prev[:half], "layer", shift(nl, 1))
    far_b = lax.ppermute(from_next[half:], "layer", shift(nl, nl - 1))
    panel = jnp.concatenate([own, from_next, far_a, far_b, from_prev], axis=0)
    rows = own.shape[0]
    width = HB * block_size
    last_at = ((nl - 1 - lidx) % nl) * rows + rows - width
    first_at = ((0 - lidx) % nl) * rows
    last = lax.dynamic_slice_in_dim(panel, last_at, width, axis=0)
    first = lax.dynamic_slice_in_dim(panel, first_at, width, axis=0)
    lo = lax.ppermute(last, "grid", shift(ng, 1))
    hi = lax.ppermute(first, "grid", shift(ng, ng - 1))
    return jnp.concatenate([panel, lo, hi], axis=0)


def step_kernel(pos_ref, h_ref, panel_ref, prev_ref, out_ref):
    rows, slots, block_size = h_ref.shape[0], h_ref.shape[1], h_ref.shape[2]
    for i in range(rows):
        acc = jnp.dot(h_ref[i, 0], panel_ref[pos_ref[i * slots]], preferred_element_type=jnp.float32)
        for s in range(1, slots):
            acc = acc + jnp.dot(h_ref[i, s], panel_ref[pos_ref[i * slots + s]], preferred_element_type=jnp.float32)
        at = slice(i * block_size, (i + 1) * block_size)
        out_ref[at, :] = (2.0 * acc - prev_ref[at, :].astype(jnp.float32)).astype(out_ref.dtype)


def own_rows(h_own, pos_flat, chunk, previous, lidx):
    block_size = h_own.shape[2]
    width = chunk.shape[1]
    tile = TILE if width % TILE == 0 else width
    wide = exchange(chunk, lidx, block_size)
    blocks = wide.reshape(wide.shape[0] // block_size, block_size, width)
    grid_spec = pltpu.PrefetchScalarGridSpec(
        num_scalar_prefetch=1,
        grid=(width // tile,),
        in_specs=[
            pl.BlockSpec(h_own.shape, lambda j, p: (0, 0, 0, 0)),
            pl.BlockSpec((blocks.shape[0], block_size, tile), lambda j, p: (0, 0, j)),
            pl.BlockSpec((chunk.shape[0], tile), lambda j, p: (0, j)),
        ],
        out_specs=pl.BlockSpec((chunk.shape[0], tile), lambda j, p: (0, j)),
    )
    return pl.pallas_call(
        step_kernel,
        grid_spec=grid_spec,
        out_shape=jax.ShapeDtypeStruct(chunk.shape, jnp.bfloat16),
        compiler_params=pltpu.CompilerParams(vmem_limit_bytes=48 * 1024 * 1024),
    )(pos_flat, h_own, blocks, previous)


def shards(h_blocks, block_cols, t_now, t_prev):
    group_rows, block_size = h_blocks.shape[0], h_blocks.shape[2]
    nl = lax.axis_size("layer")
    total_blocks = group_rows * lax.axis_size("grid")
    per_dev = group_rows // nl
    lidx = lax.axis_index("layer")
    first_block = lax.axis_index("grid") * group_rows
    rel = (block_cols - first_block + HB + total_blocks) % total_blocks

    h_split = h_blocks.reshape(nl, per_dev, *h_blocks.shape[1:])
    p_split = rel.reshape(nl, per_dev, rel.shape[1])
    h_parts = [lax.dynamic_index_in_dim(h_split, lidx, 0, keepdims=False)]
    p_parts = [lax.dynamic_index_in_dim(p_split, lidx, 0, keepdims=False)]
    for k in range(1, nl):
        dest = (lidx + k) % nl
        h_parts.append(lax.ppermute(lax.dynamic_index_in_dim(h_split, dest, 0, keepdims=False), "layer", shift(nl, k)))
        p_parts.append(lax.ppermute(lax.dynamic_index_in_dim(p_split, dest, 0, keepdims=False), "layer", shift(nl, k)))
    h_own = jnp.concatenate(h_parts, axis=1)
    rel_own = jnp.concatenate(p_parts, axis=1)
    inner = rel_own - HB
    owner = inner // per_dev
    pos_own = ((owner - lidx) % nl) * per_dev + inner % per_dev
    pos_own = jnp.where(rel_own < HB, nl * per_dev + rel_own, pos_own)
    pos_own = jnp.where(rel_own >= HB + group_rows, rel_own, pos_own)

    pos_flat = pos_own.reshape(-1).astype(jnp.int32)
    width = t_now.shape[1]
    step = width // NCH

    def recur(current, previous):
        outs = []
        for c in range(NCH):
            outs.append(own_rows(h_own, pos_flat, current[c], previous[c], lidx))
        return outs

    now_chunks = [t_now[:, c * step:(c + 1) * step] for c in range(NCH)]
    prev_chunks = [t_prev[:, c * step:(c + 1) * step] for c in range(NCH)]
    next_chunks = recur(now_chunks, prev_chunks)
    after_chunks = recur(next_chunks, now_chunks)
    return (jnp.concatenate(next_chunks, axis=1), jnp.concatenate(after_chunks, axis=1))


def solution(mesh):
    in_specs = (
        P("grid", "layer", None, None),
        P("grid", "layer"),
        P(("grid", "layer"), None),
        P(("grid", "layer"), None),
    )
    out_specs = (P(("grid", "layer"), None), P(("grid", "layer"), None))
    return jax.shard_map(shards, mesh=mesh, in_specs=in_specs, out_specs=out_specs, check_vma=False)
```

```python
import jax
import jax.numpy as jnp
from jax import lax
from jax.sharding import PartitionSpec as P
from jax.experimental import pallas as pl
from jax.experimental.pallas import tpu as pltpu

KB = 8
HB = 2
NCH = 2
TILE = 384


def shift(size, k):
    return [(i, (i + k) % size) for i in range(size)]


def exchange(own, lidx, block_size):
    nl = lax.axis_size("layer")
    ng = lax.axis_size("grid")
    half = own.shape[0] // 2
    from_prev = lax.ppermute(own, "layer", shift(nl, 1))
    from_next = lax.ppermute(own, "layer", shift(nl, nl - 1))
    far_a = lax.ppermute(from_prev[:half], "layer", shift(nl, 1))
    far_b = lax.ppermute(from_next[half:], "layer", shift(nl, nl - 1))
    panel = jnp.concatenate([own, from_next, far_a, far_b, from_prev], axis=0)
    rows = own.shape[0]
    width = HB * block_size
    flat = ("grid", "layer")
    lo = sum(lax.ppermute(own[rows - width:], flat, [(((g - 1) % ng) * nl + nl - 1, g * nl + k) for g in range(ng)]) for k in range(nl))
    hi = sum(lax.ppermute(own[:width], flat, [(((g + 1) % ng) * nl, g * nl + k) for g in range(ng)]) for k in range(nl))
    return jnp.concatenate([panel, lo, hi], axis=0)


def step_kernel(pos_ref, h_ref, panel_ref, prev_ref, out_ref):
    rows, slots, block_size = h_ref.shape[0], h_ref.shape[1], h_ref.shape[2]
    for i in range(rows):
        acc = jnp.dot(h_ref[i, 0], panel_ref[pos_ref[i * slots]], preferred_element_type=jnp.float32)
        for s in range(1, slots):
            acc = acc + jnp.dot(h_ref[i, s], panel_ref[pos_ref[i * slots + s]], preferred_element_type=jnp.float32)
        at = slice(i * block_size, (i + 1) * block_size)
        out_ref[at, :] = (2.0 * acc - prev_ref[at, :].astype(jnp.float32)).astype(out_ref.dtype)


def own_rows(h_own, pos_flat, chunk, previous, lidx):
    block_size = h_own.shape[2]
    width = chunk.shape[1]
    tile = TILE if width % TILE == 0 else width
    wide = exchange(chunk, lidx, block_size)
    blocks = wide.reshape(wide.shape[0] // block_size, block_size, width)
    grid_spec = pltpu.PrefetchScalarGridSpec(
        num_scalar_prefetch=1,
        grid=(width // tile,),
        in_specs=[
            pl.BlockSpec(h_own.shape, lambda j, p: (0, 0, 0, 0)),
            pl.BlockSpec((blocks.shape[0], block_size, tile), lambda j, p: (0, 0, j)),
            pl.BlockSpec((chunk.shape[0], tile), lambda j, p: (0, j)),
        ],
        out_specs=pl.BlockSpec((chunk.shape[0], tile), lambda j, p: (0, j)),
    )
    return pl.pallas_call(
        step_kernel,
        grid_spec=grid_spec,
        out_shape=jax.ShapeDtypeStruct(chunk.shape, jnp.bfloat16),
        compiler_params=pltpu.CompilerParams(vmem_limit_bytes=48 * 1024 * 1024),
    )(pos_flat, h_own, blocks, previous)


def shards(h_blocks, block_cols, t_now, t_prev):
    group_rows, block_size = h_blocks.shape[0], h_blocks.shape[2]
    nl = lax.axis_size("layer")
    total_blocks = group_rows * lax.axis_size("grid")
    per_dev = group_rows // nl
    lidx = lax.axis_index("layer")
    first_block = lax.axis_index("grid") * group_rows
    rel = (block_cols - first_block + HB + total_blocks) % total_blocks

    h_split = h_blocks.reshape(nl, per_dev, *h_blocks.shape[1:])
    p_split = rel.reshape(nl, per_dev, rel.shape[1])
    h_parts = [lax.dynamic_index_in_dim(h_split, lidx, 0, keepdims=False)]
    p_parts = [lax.dynamic_index_in_dim(p_split, lidx, 0, keepdims=False)]
    for k in range(1, nl):
        dest = (lidx + k) % nl
        h_parts.append(lax.ppermute(lax.dynamic_index_in_dim(h_split, dest, 0, keepdims=False), "layer", shift(nl, k)))
        p_parts.append(lax.ppermute(lax.dynamic_index_in_dim(p_split, dest, 0, keepdims=False), "layer", shift(nl, k)))
    h_own = jnp.concatenate(h_parts, axis=1)
    rel_own = jnp.concatenate(p_parts, axis=1)
    inner = rel_own - HB
    owner = inner // per_dev
    pos_own = ((owner - lidx) % nl) * per_dev + inner % per_dev
    pos_own = jnp.where(rel_own < HB, nl * per_dev + rel_own, pos_own)
    pos_own = jnp.where(rel_own >= HB + group_rows, rel_own, pos_own)

    pos_flat = pos_own.reshape(-1).astype(jnp.int32)
    width = t_now.shape[1]
    step = width // NCH

    def recur(current, previous):
        outs = []
        for c in range(NCH):
            outs.append(own_rows(h_own, pos_flat, current[c], previous[c], lidx))
        return outs

    now_chunks = [t_now[:, c * step:(c + 1) * step] for c in range(NCH)]
    prev_chunks = [t_prev[:, c * step:(c + 1) * step] for c in range(NCH)]
    next_chunks = recur(now_chunks, prev_chunks)
    after_chunks = recur(next_chunks, now_chunks)
    return (jnp.concatenate(next_chunks, axis=1), jnp.concatenate(after_chunks, axis=1))


def solution(mesh):
    in_specs = (
        P("grid", "layer", None, None),
        P("grid", "layer"),
        P(("grid", "layer"), None),
        P(("grid", "layer"), None),
    )
    out_specs = (P(("grid", "layer"), None), P(("grid", "layer"), None))
    return jax.shard_map(shards, mesh=mesh, in_specs=in_specs, out_specs=out_specs, check_vma=False)
```

```python
import jax
import jax.numpy as jnp
from jax import lax
from jax.sharding import PartitionSpec as P
from jax.experimental import pallas as pl
from jax.experimental.pallas import tpu as pltpu

KB = 8
HB = 2
NCH = 3
TILE = 256


def shift(size, k):
    return [(i, (i + k) % size) for i in range(size)]


def exchange(own, lidx, block_size):
    nl = lax.axis_size("layer")
    ng = lax.axis_size("grid")
    half = own.shape[0] // 2
    from_prev = lax.ppermute(own, "layer", shift(nl, 1))
    from_next = lax.ppermute(own, "layer", shift(nl, nl - 1))
    far_a = lax.ppermute(from_prev[:half], "layer", shift(nl, 1))
    far_b = lax.ppermute(from_next[half:], "layer", shift(nl, nl - 1))
    panel = jnp.concatenate([own, from_next, far_a, far_b, from_prev], axis=0)
    rows = own.shape[0]
    width = HB * block_size
    last_at = ((nl - 1 - lidx) % nl) * rows + rows - width
    first_at = ((0 - lidx) % nl) * rows
    last = lax.dynamic_slice_in_dim(panel, last_at, width, axis=0)
    first = lax.dynamic_slice_in_dim(panel, first_at, width, axis=0)
    lo = lax.ppermute(last, "grid", shift(ng, 1))
    hi = lax.ppermute(first, "grid", shift(ng, ng - 1))
    return jnp.concatenate([panel, lo, hi], axis=0)


def step_kernel(pos_ref, h_ref, panel_ref, prev_ref, out_ref):
    rows, slots, block_size = h_ref.shape[0], h_ref.shape[1], h_ref.shape[2]
    for i in range(rows):
        acc = jnp.dot(h_ref[i, 0], panel_ref[pos_ref[i * slots]], preferred_element_type=jnp.float32)
        for s in range(1, slots):
            acc = acc + jnp.dot(h_ref[i, s], panel_ref[pos_ref[i * slots + s]], preferred_element_type=jnp.float32)
        at = slice(i * block_size, (i + 1) * block_size)
        out_ref[at, :] = (2.0 * acc - prev_ref[at, :].astype(jnp.float32)).astype(out_ref.dtype)


def own_rows(h_own, pos_flat, chunk, previous, lidx):
    block_size = h_own.shape[2]
    width = chunk.shape[1]
    tile = TILE if width % TILE == 0 else width
    wide = exchange(chunk, lidx, block_size)
    blocks = wide.reshape(wide.shape[0] // block_size, block_size, width)
    grid_spec = pltpu.PrefetchScalarGridSpec(
        num_scalar_prefetch=1,
        grid=(width // tile,),
        in_specs=[
            pl.BlockSpec(h_own.shape, lambda j, p: (0, 0, 0, 0)),
            pl.BlockSpec((blocks.shape[0], block_size, tile), lambda j, p: (0, 0, j)),
            pl.BlockSpec((chunk.shape[0], tile), lambda j, p: (0, j)),
        ],
        out_specs=pl.BlockSpec((chunk.shape[0], tile), lambda j, p: (0, j)),
    )
    return pl.pallas_call(
        step_kernel,
        grid_spec=grid_spec,
        out_shape=jax.ShapeDtypeStruct(chunk.shape, jnp.bfloat16),
        compiler_params=pltpu.CompilerParams(vmem_limit_bytes=48 * 1024 * 1024),
    )(pos_flat, h_own, blocks, previous)


def shards(h_blocks, block_cols, t_now, t_prev):
    group_rows, block_size = h_blocks.shape[0], h_blocks.shape[2]
    nl = lax.axis_size("layer")
    total_blocks = group_rows * lax.axis_size("grid")
    per_dev = group_rows // nl
    lidx = lax.axis_index("layer")
    first_block = lax.axis_index("grid") * group_rows
    rel = (block_cols - first_block + HB + total_blocks) % total_blocks

    h_split = h_blocks.reshape(nl, per_dev, *h_blocks.shape[1:])
    p_split = rel.reshape(nl, per_dev, rel.shape[1])
    h_parts = [lax.dynamic_index_in_dim(h_split, lidx, 0, keepdims=False)]
    p_parts = [lax.dynamic_index_in_dim(p_split, lidx, 0, keepdims=False)]
    for k in range(1, nl):
        dest = (lidx + k) % nl
        h_parts.append(lax.ppermute(lax.dynamic_index_in_dim(h_split, dest, 0, keepdims=False), "layer", shift(nl, k)))
        p_parts.append(lax.ppermute(lax.dynamic_index_in_dim(p_split, dest, 0, keepdims=False), "layer", shift(nl, k)))
    h_own = jnp.concatenate(h_parts, axis=1)
    rel_own = jnp.concatenate(p_parts, axis=1)
    inner = rel_own - HB
    owner = inner // per_dev
    pos_own = ((owner - lidx) % nl) * per_dev + inner % per_dev
    pos_own = jnp.where(rel_own < HB, nl * per_dev + rel_own, pos_own)
    pos_own = jnp.where(rel_own >= HB + group_rows, rel_own, pos_own)

    pos_flat = pos_own.reshape(-1).astype(jnp.int32)
    width = t_now.shape[1]
    step = width // NCH

    def recur(current, previous):
        outs = []
        for c in range(NCH):
            outs.append(own_rows(h_own, pos_flat, current[c], previous[c], lidx))
        return outs

    now_chunks = [t_now[:, c * step:(c + 1) * step] for c in range(NCH)]
    prev_chunks = [t_prev[:, c * step:(c + 1) * step] for c in range(NCH)]
    next_chunks = recur(now_chunks, prev_chunks)
    after_chunks = recur(next_chunks, now_chunks)
    return (jnp.concatenate(next_chunks, axis=1), jnp.concatenate(after_chunks, axis=1))


def solution(mesh):
    in_specs = (
        P("grid", "layer", None, None),
        P("grid", "layer"),
        P(("grid", "layer"), None),
        P(("grid", "layer"), None),
    )
    out_specs = (P(("grid", "layer"), None), P(("grid", "layer"), None))
    return jax.shard_map(shards, mesh=mesh, in_specs=in_specs, out_specs=out_specs, check_vma=False)
```

```python
import jax
import jax.numpy as jnp
from jax import lax
from jax.sharding import PartitionSpec as P
from jax.experimental import pallas as pl
from jax.experimental.pallas import tpu as pltpu

KB = 8
HB = 2
NCH = 2
TILE = 384


def shift(size, k):
    return [(i, (i + k) % size) for i in range(size)]


def exchange(own, lidx, block_size):
    nl = lax.axis_size("layer")
    ng = lax.axis_size("grid")
    half = own.shape[0] // 2
    from_prev = lax.ppermute(own, "layer", shift(nl, 1))
    from_next = lax.ppermute(own, "layer", shift(nl, nl - 1))
    far_a = lax.ppermute(from_prev[:half], "layer", shift(nl, 1))
    far_b = lax.ppermute(from_next[half:], "layer", shift(nl, nl - 1))
    panel = jnp.concatenate([own, from_next, far_a, far_b, from_prev], axis=0)
    rows = own.shape[0]
    width = HB * block_size
    last_at = ((nl - 1 - lidx) % nl) * rows + rows - width
    first_at = ((0 - lidx) % nl) * rows
    last = lax.dynamic_slice_in_dim(panel, last_at, width, axis=0)
    first = lax.dynamic_slice_in_dim(panel, first_at, width, axis=0)
    lo = lax.ppermute(last, "grid", shift(ng, 1))
    hi = lax.ppermute(first, "grid", shift(ng, ng - 1))
    return jnp.concatenate([panel, lo, hi], axis=0)


def step_kernel(pos_ref, h_ref, panel_ref, prev_ref, out_ref):
    rows, slots, block_size = h_ref.shape[0], h_ref.shape[1], h_ref.shape[2]
    for i in range(rows):
        acc = jnp.dot(h_ref[i, 0], panel_ref[pos_ref[i * slots]], preferred_element_type=jnp.float32)
        for s in range(1, slots):
            acc = acc + jnp.dot(h_ref[i, s], panel_ref[pos_ref[i * slots + s]], preferred_element_type=jnp.float32)
        at = slice(i * block_size, (i + 1) * block_size)
        out_ref[at, :] = (2.0 * acc - prev_ref[at, :].astype(jnp.float32)).astype(out_ref.dtype)


def own_rows(h_own, pos_flat, chunk, previous, lidx):
    block_size = h_own.shape[2]
    width = chunk.shape[1]
    tile = TILE if width % TILE == 0 else width
    wide = exchange(chunk, lidx, block_size)
    blocks = wide.reshape(wide.shape[0] // block_size, block_size, width)
    grid_spec = pltpu.PrefetchScalarGridSpec(
        num_scalar_prefetch=1,
        grid=(width // tile,),
        in_specs=[
            pl.BlockSpec(h_own.shape, lambda j, p: (0, 0, 0, 0)),
            pl.BlockSpec((blocks.shape[0], block_size, tile), lambda j, p: (0, 0, j)),
            pl.BlockSpec((chunk.shape[0], tile), lambda j, p: (0, j)),
        ],
        out_specs=pl.BlockSpec((chunk.shape[0], tile), lambda j, p: (0, j)),
    )
    return pl.pallas_call(
        step_kernel,
        grid_spec=grid_spec,
        out_shape=jax.ShapeDtypeStruct(chunk.shape, jnp.bfloat16),
        compiler_params=pltpu.CompilerParams(vmem_limit_bytes=48 * 1024 * 1024),
    )(pos_flat, h_own, blocks, previous)


def shards(h_blocks, block_cols, t_now, t_prev):
    group_rows, block_size = h_blocks.shape[0], h_blocks.shape[2]
    nl = lax.axis_size("layer")
    total_blocks = group_rows * lax.axis_size("grid")
    per_dev = group_rows // nl
    lidx = lax.axis_index("layer")
    first_block = lax.axis_index("grid") * group_rows
    rel = (block_cols - first_block + HB + total_blocks) % total_blocks

    h_split = h_blocks.reshape(nl, per_dev, *h_blocks.shape[1:])
    p_split = rel.reshape(nl, per_dev, rel.shape[1])
    h_parts = [lax.dynamic_index_in_dim(h_split, lidx, 0, keepdims=False)]
    p_parts = [lax.dynamic_index_in_dim(p_split, lidx, 0, keepdims=False)]
    for k in range(1, nl):
        dest = (lidx + k) % nl
        h_parts.append(lax.ppermute(lax.dynamic_index_in_dim(h_split, dest, 0, keepdims=False), "layer", shift(nl, k)))
        p_parts.append(lax.ppermute(lax.dynamic_index_in_dim(p_split, dest, 0, keepdims=False), "layer", shift(nl, k)))
    h_own = jnp.concatenate(h_parts, axis=1)
    rel_own = jnp.concatenate(p_parts, axis=1)
    t_now, h_own, rel_own = lax.optimization_barrier((t_now, h_own, rel_own))
    inner = rel_own - HB
    owner = inner // per_dev
    pos_own = ((owner - lidx) % nl) * per_dev + inner % per_dev
    pos_own = jnp.where(rel_own < HB, nl * per_dev + rel_own, pos_own)
    pos_own = jnp.where(rel_own >= HB + group_rows, rel_own, pos_own)

    pos_flat = pos_own.reshape(-1).astype(jnp.int32)
    width = t_now.shape[1]
    step = width // NCH

    def recur(current, previous):
        outs = []
        for c in range(NCH):
            outs.append(own_rows(h_own, pos_flat, current[c], previous[c], lidx))
        return outs

    now_chunks = [t_now[:, c * step:(c + 1) * step] for c in range(NCH)]
    prev_chunks = [t_prev[:, c * step:(c + 1) * step] for c in range(NCH)]
    next_chunks = recur(now_chunks, prev_chunks)
    after_chunks = recur(next_chunks, now_chunks)
    return (jnp.concatenate(next_chunks, axis=1), jnp.concatenate(after_chunks, axis=1))


def solution(mesh):
    in_specs = (
        P("grid", "layer", None, None),
        P("grid", "layer"),
        P(("grid", "layer"), None),
        P(("grid", "layer"), None),
    )
    out_specs = (P(("grid", "layer"), None), P(("grid", "layer"), None))
    return jax.shard_map(shards, mesh=mesh, in_specs=in_specs, out_specs=out_specs, check_vma=False)
```

```python
import jax
import jax.numpy as jnp
from jax import lax
from jax.sharding import PartitionSpec as P
from jax.experimental import pallas as pl
from jax.experimental.pallas import tpu as pltpu

KB = 8
HB = 2
NCH = 2
TILE = 384


def shift(size, k):
    return [(i, (i + k) % size) for i in range(size)]


def exchange(own, lidx, block_size):
    nl = lax.axis_size("layer")
    ng = lax.axis_size("grid")
    half = own.shape[0] // 2
    from_prev = lax.ppermute(own, "layer", shift(nl, 1))
    from_next = lax.ppermute(own, "layer", shift(nl, nl - 1))
    far_a = lax.ppermute(from_prev[:half], "layer", shift(nl, 1))
    far_b = lax.ppermute(from_next[half:], "layer", shift(nl, nl - 1))
    panel = jnp.concatenate([own, from_next, far_a, far_b, from_prev], axis=0)
    rows = own.shape[0]
    width = HB * block_size
    last_at = ((nl - 1 - lidx) % nl) * rows + rows - width
    first_at = ((0 - lidx) % nl) * rows
    last = lax.dynamic_slice_in_dim(panel, last_at, width, axis=0)
    first = lax.dynamic_slice_in_dim(panel, first_at, width, axis=0)
    lo = lax.ppermute(last, "grid", shift(ng, 1))
    hi = lax.ppermute(first, "grid", shift(ng, ng - 1))
    return jnp.concatenate([panel, lo, hi], axis=0)


def step_kernel(pos_ref, h_ref, panel_ref, prev_ref, out_ref):
    rows, slots, block_size = h_ref.shape[0], h_ref.shape[1], h_ref.shape[2]
    for i in range(rows):
        acc = jnp.dot(h_ref[i, 0], panel_ref[pos_ref[i * slots]], preferred_element_type=jnp.float32)
        for s in range(1, slots):
            acc = acc + jnp.dot(h_ref[i, s], panel_ref[pos_ref[i * slots + s]], preferred_element_type=jnp.float32)
        at = slice(i * block_size, (i + 1) * block_size)
        out_ref[at, :] = (2.0 * acc - prev_ref[at, :].astype(jnp.float32)).astype(out_ref.dtype)


def own_rows(h_own, pos_flat, chunk, previous, lidx):
    block_size = h_own.shape[2]
    width = chunk.shape[1]
    tile = TILE if width % TILE == 0 else width
    wide = exchange(chunk, lidx, block_size)
    blocks = wide.reshape(wide.shape[0] // block_size, block_size, width)
    grid_spec = pltpu.PrefetchScalarGridSpec(
        num_scalar_prefetch=1,
        grid=(width // tile,),
        in_specs=[
            pl.BlockSpec(h_own.shape, lambda j, p: (0, 0, 0, 0)),
            pl.BlockSpec((blocks.shape[0], block_size, tile), lambda j, p: (0, 0, j)),
            pl.BlockSpec((chunk.shape[0], tile), lambda j, p: (0, j)),
        ],
        out_specs=pl.BlockSpec((chunk.shape[0], tile), lambda j, p: (0, j)),
    )
    return pl.pallas_call(
        step_kernel,
        grid_spec=grid_spec,
        out_shape=jax.ShapeDtypeStruct(chunk.shape, jnp.bfloat16),
        compiler_params=pltpu.CompilerParams(vmem_limit_bytes=48 * 1024 * 1024),
    )(pos_flat, h_own, blocks, previous)


def shards(h_blocks, block_cols, t_now, t_prev):
    group_rows, block_size = h_blocks.shape[0], h_blocks.shape[2]
    nl = lax.axis_size("layer")
    total_blocks = group_rows * lax.axis_size("grid")
    per_dev = group_rows // nl
    lidx = lax.axis_index("layer")
    first_block = lax.axis_index("grid") * group_rows
    rel = (block_cols - first_block + HB + total_blocks) % total_blocks

    h_split = h_blocks.reshape(nl, per_dev, *h_blocks.shape[1:])
    p_split = rel.reshape(nl, per_dev, rel.shape[1])
    h_parts = [lax.dynamic_index_in_dim(h_split, lidx, 0, keepdims=False)]
    p_parts = [lax.dynamic_index_in_dim(p_split, lidx, 0, keepdims=False)]
    for k in range(1, nl):
        dest = (lidx + k) % nl
        h_parts.append(lax.ppermute(lax.dynamic_index_in_dim(h_split, dest, 0, keepdims=False), "layer", shift(nl, k)))
        p_parts.append(lax.ppermute(lax.dynamic_index_in_dim(p_split, dest, 0, keepdims=False), "layer", shift(nl, k)))
    h_own = jnp.concatenate(h_parts, axis=1)
    rel_own = jnp.concatenate(p_parts, axis=1)
    t_now, rel_own = lax.optimization_barrier((t_now, rel_own))
    inner = rel_own - HB
    owner = inner // per_dev
    pos_own = ((owner - lidx) % nl) * per_dev + inner % per_dev
    pos_own = jnp.where(rel_own < HB, nl * per_dev + rel_own, pos_own)
    pos_own = jnp.where(rel_own >= HB + group_rows, rel_own, pos_own)

    pos_flat = pos_own.reshape(-1).astype(jnp.int32)
    width = t_now.shape[1]
    step = width // NCH

    def recur(current, previous):
        outs = []
        for c in range(NCH):
            outs.append(own_rows(h_own, pos_flat, current[c], previous[c], lidx))
        return outs

    now_chunks = [t_now[:, c * step:(c + 1) * step] for c in range(NCH)]
    prev_chunks = [t_prev[:, c * step:(c + 1) * step] for c in range(NCH)]
    next_chunks = recur(now_chunks, prev_chunks)
    after_chunks = recur(next_chunks, now_chunks)
    return (jnp.concatenate(next_chunks, axis=1), jnp.concatenate(after_chunks, axis=1))


def solution(mesh):
    in_specs = (
        P("grid", "layer", None, None),
        P("grid", "layer"),
        P(("grid", "layer"), None),
        P(("grid", "layer"), None),
    )
    out_specs = (P(("grid", "layer"), None), P(("grid", "layer"), None))
    return jax.shard_map(shards, mesh=mesh, in_specs=in_specs, out_specs=out_specs, check_vma=False)
```

```python
import jax
import jax.numpy as jnp
from jax import lax
from jax.sharding import PartitionSpec as P
from jax.experimental import pallas as pl
from jax.experimental.pallas import tpu as pltpu

KB = 8
HB = 2
NCH = 2
TILE = 384


def shift(size, k):
    return [(i, (i + k) % size) for i in range(size)]


def exchange(own, lidx, block_size):
    nl = lax.axis_size("layer")
    ng = lax.axis_size("grid")
    half = own.shape[0] // 2
    from_prev = lax.ppermute(own, "layer", shift(nl, 1))
    from_next = lax.ppermute(own, "layer", shift(nl, nl - 1))
    far_a = lax.ppermute(from_prev[:half], "layer", shift(nl, 1))
    far_b = lax.ppermute(from_next[half:], "layer", shift(nl, nl - 1))
    panel = jnp.concatenate([own, from_next, far_a, far_b, from_prev], axis=0)
    rows = own.shape[0]
    width = HB * block_size
    last_at = ((nl - 1 - lidx) % nl) * rows + rows - width
    first_at = ((0 - lidx) % nl) * rows
    last = lax.dynamic_slice_in_dim(panel, last_at, width, axis=0)
    first = lax.dynamic_slice_in_dim(panel, first_at, width, axis=0)
    lo = lax.ppermute(last, "grid", shift(ng, 1))
    hi = lax.ppermute(first, "grid", shift(ng, ng - 1))
    return jnp.concatenate([panel, lo, hi], axis=0)


def step_kernel(pos_ref, h_ref, panel_ref, prev_ref, out_ref):
    rows, slots, block_size = h_ref.shape[0], h_ref.shape[1], h_ref.shape[2]
    for i in range(rows):
        acc = jnp.dot(h_ref[i, 0], panel_ref[pos_ref[i * slots]], preferred_element_type=jnp.float32)
        for s in range(1, slots):
            acc = acc + jnp.dot(h_ref[i, s], panel_ref[pos_ref[i * slots + s]], preferred_element_type=jnp.float32)
        at = slice(i * block_size, (i + 1) * block_size)
        out_ref[at, :] = (2.0 * acc - prev_ref[at, :].astype(jnp.float32)).astype(out_ref.dtype)


def own_rows(h_own, pos_flat, chunk, previous, lidx):
    block_size = h_own.shape[2]
    width = chunk.shape[1]
    tile = TILE if width % TILE == 0 else width
    wide = exchange(chunk, lidx, block_size)
    blocks = wide.reshape(wide.shape[0] // block_size, block_size, width)
    grid_spec = pltpu.PrefetchScalarGridSpec(
        num_scalar_prefetch=1,
        grid=(width // tile,),
        in_specs=[
            pl.BlockSpec(h_own.shape, lambda j, p: (0, 0, 0, 0)),
            pl.BlockSpec((blocks.shape[0], block_size, tile), lambda j, p: (0, 0, j)),
            pl.BlockSpec((chunk.shape[0], tile), lambda j, p: (0, j)),
        ],
        out_specs=pl.BlockSpec((chunk.shape[0], tile), lambda j, p: (0, j)),
    )
    return pl.pallas_call(
        step_kernel,
        grid_spec=grid_spec,
        out_shape=jax.ShapeDtypeStruct(chunk.shape, jnp.bfloat16),
        compiler_params=pltpu.CompilerParams(vmem_limit_bytes=48 * 1024 * 1024),
    )(pos_flat, h_own, blocks, previous)


def shards(h_blocks, block_cols, t_now, t_prev):
    group_rows, block_size = h_blocks.shape[0], h_blocks.shape[2]
    nl = lax.axis_size("layer")
    total_blocks = group_rows * lax.axis_size("grid")
    per_dev = group_rows // nl
    lidx = lax.axis_index("layer")
    first_block = lax.axis_index("grid") * group_rows
    rel = (block_cols - first_block + HB + total_blocks) % total_blocks

    h_split = h_blocks.reshape(nl, per_dev, *h_blocks.shape[1:])
    p_split = rel.reshape(nl, per_dev, rel.shape[1])
    h_parts = [lax.dynamic_index_in_dim(h_split, lidx, 0, keepdims=False)]
    p_parts = [lax.dynamic_index_in_dim(p_split, lidx, 0, keepdims=False)]
    h_size = h_parts[0].size
    for k in range(1, nl):
        dest = (lidx + k) % nl
        piece = jnp.concatenate([
            lax.dynamic_index_in_dim(h_split, dest, 0, keepdims=False).reshape(-1),
            lax.dynamic_index_in_dim(p_split, dest, 0, keepdims=False).reshape(-1).astype(h_blocks.dtype),
        ])
        got = lax.ppermute(piece, "layer", shift(nl, k))
        h_parts.append(got[:h_size].reshape(h_parts[0].shape))
        p_parts.append(got[h_size:].astype(p_split.dtype).reshape(p_parts[0].shape))
    h_own = jnp.concatenate(h_parts, axis=1)
    rel_own = jnp.concatenate(p_parts, axis=1)
    t_now, rel_own = lax.optimization_barrier((t_now, rel_own))
    inner = rel_own - HB
    owner = inner // per_dev
    pos_own = ((owner - lidx) % nl) * per_dev + inner % per_dev
    pos_own = jnp.where(rel_own < HB, nl * per_dev + rel_own, pos_own)
    pos_own = jnp.where(rel_own >= HB + group_rows, rel_own, pos_own)

    pos_flat = pos_own.reshape(-1).astype(jnp.int32)
    width = t_now.shape[1]
    step = width // NCH

    def recur(current, previous):
        outs = []
        for c in range(NCH):
            outs.append(own_rows(h_own, pos_flat, current[c], previous[c], lidx))
        return outs

    now_chunks = [t_now[:, c * step:(c + 1) * step] for c in range(NCH)]
    prev_chunks = [t_prev[:, c * step:(c + 1) * step] for c in range(NCH)]
    next_chunks = recur(now_chunks, prev_chunks)
    after_chunks = recur(next_chunks, now_chunks)
    return (jnp.concatenate(next_chunks, axis=1), jnp.concatenate(after_chunks, axis=1))


def solution(mesh):
    in_specs = (
        P("grid", "layer", None, None),
        P("grid", "layer"),
        P(("grid", "layer"), None),
        P(("grid", "layer"), None),
    )
    out_specs = (P(("grid", "layer"), None), P(("grid", "layer"), None))
    return jax.shard_map(shards, mesh=mesh, in_specs=in_specs, out_specs=out_specs, check_vma=False)
```

```python
import jax
import jax.numpy as jnp
from jax import lax
from jax.sharding import PartitionSpec as P
from jax.experimental import pallas as pl
from jax.experimental.pallas import tpu as pltpu

KB = 8
HB = 2
NCH = 2
TILE = 384


def shift(size, k):
    return [(i, (i + k) % size) for i in range(size)]


def exchange(own, lidx, block_size):
    nl = lax.axis_size("layer")
    ng = lax.axis_size("grid")
    half = own.shape[0] // 2
    from_prev = lax.ppermute(own, "layer", shift(nl, 1))
    from_next = lax.ppermute(own, "layer", shift(nl, nl - 1))
    far_a = lax.ppermute(from_prev[:half], "layer", shift(nl, 1))
    far_b = lax.ppermute(from_next[half:], "layer", shift(nl, nl - 1))
    panel = jnp.concatenate([own, from_next, far_a, far_b, from_prev], axis=0)
    rows = own.shape[0]
    width = HB * block_size
    last_at = ((nl - 1 - lidx) % nl) * rows + rows - width
    first_at = ((0 - lidx) % nl) * rows
    last = lax.dynamic_slice_in_dim(panel, last_at, width, axis=0)
    first = lax.dynamic_slice_in_dim(panel, first_at, width, axis=0)
    lo = lax.ppermute(last, "grid", shift(ng, 1))
    hi = lax.ppermute(first, "grid", shift(ng, ng - 1))
    return jnp.concatenate([panel, lo, hi], axis=0)


def step_kernel(pos_ref, h_ref, panel_ref, prev_ref, *refs):
    out_ref = refs[-1]
    rows, slots, block_size = h_ref.shape[0], h_ref.shape[1], h_ref.shape[2]
    for i in range(rows):
        acc = jnp.dot(h_ref[i, 0], panel_ref[pos_ref[i * slots]], preferred_element_type=jnp.float32)
        for s in range(1, slots):
            acc = acc + jnp.dot(h_ref[i, s], panel_ref[pos_ref[i * slots + s]], preferred_element_type=jnp.float32)
        at = slice(i * block_size, (i + 1) * block_size)
        out_ref[at, :] = (2.0 * acc - prev_ref[at, :].astype(jnp.float32)).astype(out_ref.dtype)


def own_rows(h_own, pos_flat, chunk, previous, lidx, into=None, at=0):
    block_size = h_own.shape[2]
    width = chunk.shape[1]
    tile = TILE if width % TILE == 0 else width
    wide = exchange(chunk, lidx, block_size)
    blocks = wide.reshape(wide.shape[0] // block_size, block_size, width)
    in_specs = [
        pl.BlockSpec(h_own.shape, lambda j, p: (0, 0, 0, 0)),
        pl.BlockSpec((blocks.shape[0], block_size, tile), lambda j, p: (0, 0, j)),
        pl.BlockSpec((chunk.shape[0], tile), lambda j, p: (0, j)),
    ]
    args = [pos_flat, h_own, blocks, previous]
    out_shape = jax.ShapeDtypeStruct(chunk.shape, jnp.bfloat16)
    out_spec = pl.BlockSpec((chunk.shape[0], tile), lambda j, p: (0, j))
    aliases = {}
    if into is not None:
        in_specs.append(pl.BlockSpec(memory_space=pl.ANY))
        args.append(into)
        aliases = {len(args) - 1: 0}
        out_shape = jax.ShapeDtypeStruct(into.shape, jnp.bfloat16)
        out_spec = pl.BlockSpec((chunk.shape[0], tile), lambda j, p: (0, at + j))
    grid_spec = pltpu.PrefetchScalarGridSpec(
        num_scalar_prefetch=1,
        grid=(width // tile,),
        in_specs=in_specs,
        out_specs=out_spec,
    )
    return pl.pallas_call(
        step_kernel,
        grid_spec=grid_spec,
        out_shape=out_shape,
        input_output_aliases=aliases,
        compiler_params=pltpu.CompilerParams(vmem_limit_bytes=48 * 1024 * 1024),
    )(*args)


def shards(h_blocks, block_cols, t_now, t_prev):
    group_rows, block_size = h_blocks.shape[0], h_blocks.shape[2]
    nl = lax.axis_size("layer")
    total_blocks = group_rows * lax.axis_size("grid")
    per_dev = group_rows // nl
    lidx = lax.axis_index("layer")
    first_block = lax.axis_index("grid") * group_rows
    rel = (block_cols - first_block + HB + total_blocks) % total_blocks

    h_split = h_blocks.reshape(nl, per_dev, *h_blocks.shape[1:])
    p_split = rel.reshape(nl, per_dev, rel.shape[1])
    h_parts = [lax.dynamic_index_in_dim(h_split, lidx, 0, keepdims=False)]
    p_parts = [lax.dynamic_index_in_dim(p_split, lidx, 0, keepdims=False)]
    for k in range(1, nl):
        dest = (lidx + k) % nl
        h_parts.append(lax.ppermute(lax.dynamic_index_in_dim(h_split, dest, 0, keepdims=False), "layer", shift(nl, k)))
        p_parts.append(lax.ppermute(lax.dynamic_index_in_dim(p_split, dest, 0, keepdims=False), "layer", shift(nl, k)))
    h_own = jnp.concatenate(h_parts, axis=1)
    rel_own = jnp.concatenate(p_parts, axis=1)
    t_now, rel_own = lax.optimization_barrier((t_now, rel_own))
    inner = rel_own - HB
    owner = inner // per_dev
    pos_own = ((owner - lidx) % nl) * per_dev + inner % per_dev
    pos_own = jnp.where(rel_own < HB, nl * per_dev + rel_own, pos_own)
    pos_own = jnp.where(rel_own >= HB + group_rows, rel_own, pos_own)

    pos_flat = pos_own.reshape(-1).astype(jnp.int32)
    width = t_now.shape[1]
    step = width // NCH

    def recur(current, previous):
        outs = []
        for c in range(NCH):
            outs.append(own_rows(h_own, pos_flat, current[c], previous[c], lidx))
        return outs

    now_chunks = [t_now[:, c * step:(c + 1) * step] for c in range(NCH)]
    prev_chunks = [t_prev[:, c * step:(c + 1) * step] for c in range(NCH)]
    next_chunks = recur(now_chunks, prev_chunks)
    after_term = jnp.zeros(t_now.shape, jnp.bfloat16)
    for c in range(NCH):
        tiles = step // (TILE if step % TILE == 0 else step)
        after_term = own_rows(h_own, pos_flat, next_chunks[c], now_chunks[c], lidx, after_term, c * tiles)
    return (jnp.concatenate(next_chunks, axis=1), after_term)


def solution(mesh):
    in_specs = (
        P("grid", "layer", None, None),
        P("grid", "layer"),
        P(("grid", "layer"), None),
        P(("grid", "layer"), None),
    )
    out_specs = (P(("grid", "layer"), None), P(("grid", "layer"), None))
    return jax.shard_map(shards, mesh=mesh, in_specs=in_specs, out_specs=out_specs, check_vma=False)
```

```python
import jax
import jax.numpy as jnp
from jax import lax
from jax.sharding import PartitionSpec as P
from jax.experimental import pallas as pl
from jax.experimental.pallas import tpu as pltpu

KB = 8
HB = 2
NCH = 2
TILE = 384


def shift(size, k):
    return [(i, (i + k) % size) for i in range(size)]


def exchange(own, lidx, block_size):
    nl = lax.axis_size("layer")
    ng = lax.axis_size("grid")
    half = own.shape[0] // 2
    from_prev = lax.ppermute(own, "layer", shift(nl, 1))
    from_next = lax.ppermute(own, "layer", shift(nl, nl - 1))
    far_a = lax.ppermute(from_prev[:half], "layer", shift(nl, 1))
    far_b = lax.ppermute(from_next[half:], "layer", shift(nl, nl - 1))
    panel = jnp.concatenate([own, from_next, far_a, far_b, from_prev], axis=0)
    rows = own.shape[0]
    width = HB * block_size
    last_at = ((nl - 1 - lidx) % nl) * rows + rows - width
    first_at = ((0 - lidx) % nl) * rows
    last = lax.dynamic_slice_in_dim(panel, last_at, width, axis=0)
    first = lax.dynamic_slice_in_dim(panel, first_at, width, axis=0)
    lo = lax.ppermute(last, "grid", shift(ng, 1))
    hi = lax.ppermute(first, "grid", shift(ng, ng - 1))
    return jnp.concatenate([panel, lo, hi], axis=0)


def step_kernel(pos_ref, h_ref, panel_ref, prev_ref, out_ref):
    slots = h_ref.shape[1]
    row = pl.program_id(1)
    acc = jnp.dot(h_ref[0, 0], panel_ref[pos_ref[row * slots]], preferred_element_type=jnp.float32)
    for s in range(1, slots):
        acc = acc + jnp.dot(h_ref[0, s], panel_ref[pos_ref[row * slots + s]], preferred_element_type=jnp.float32)
    out_ref[...] = (2.0 * acc - prev_ref[...].astype(jnp.float32)).astype(out_ref.dtype)


def own_rows(h_own, pos_flat, chunk, previous, lidx):
    block_size = h_own.shape[2]
    width = chunk.shape[1]
    tile = TILE if width % TILE == 0 else width
    wide = exchange(chunk, lidx, block_size)
    blocks = wide.reshape(wide.shape[0] // block_size, block_size, width)
    grid_spec = pltpu.PrefetchScalarGridSpec(
        num_scalar_prefetch=1,
        grid=(width // tile, h_own.shape[0]),
        in_specs=[
            pl.BlockSpec((1, *h_own.shape[1:]), lambda j, i, p: (i, 0, 0, 0)),
            pl.BlockSpec((blocks.shape[0], block_size, tile), lambda j, i, p: (0, 0, j)),
            pl.BlockSpec((block_size, tile), lambda j, i, p: (i, j)),
        ],
        out_specs=pl.BlockSpec((block_size, tile), lambda j, i, p: (i, j)),
    )
    return pl.pallas_call(
        step_kernel,
        grid_spec=grid_spec,
        out_shape=jax.ShapeDtypeStruct(chunk.shape, jnp.bfloat16),
        compiler_params=pltpu.CompilerParams(vmem_limit_bytes=48 * 1024 * 1024),
    )(pos_flat, h_own, blocks, previous)


def shards(h_blocks, block_cols, t_now, t_prev):
    group_rows, block_size = h_blocks.shape[0], h_blocks.shape[2]
    nl = lax.axis_size("layer")
    total_blocks = group_rows * lax.axis_size("grid")
    per_dev = group_rows // nl
    lidx = lax.axis_index("layer")
    first_block = lax.axis_index("grid") * group_rows
    rel = (block_cols - first_block + HB + total_blocks) % total_blocks

    h_split = h_blocks.reshape(nl, per_dev, *h_blocks.shape[1:])
    p_split = rel.reshape(nl, per_dev, rel.shape[1])
    h_parts = [lax.dynamic_index_in_dim(h_split, lidx, 0, keepdims=False)]
    p_parts = [lax.dynamic_index_in_dim(p_split, lidx, 0, keepdims=False)]
    for k in range(1, nl):
        dest = (lidx + k) % nl
        h_parts.append(lax.ppermute(lax.dynamic_index_in_dim(h_split, dest, 0, keepdims=False), "layer", shift(nl, k)))
        p_parts.append(lax.ppermute(lax.dynamic_index_in_dim(p_split, dest, 0, keepdims=False), "layer", shift(nl, k)))
    h_own = jnp.concatenate(h_parts, axis=1)
    rel_own = jnp.concatenate(p_parts, axis=1)
    t_now, rel_own = lax.optimization_barrier((t_now, rel_own))
    inner = rel_own - HB
    owner = inner // per_dev
    pos_own = ((owner - lidx) % nl) * per_dev + inner % per_dev
    pos_own = jnp.where(rel_own < HB, nl * per_dev + rel_own, pos_own)
    pos_own = jnp.where(rel_own >= HB + group_rows, rel_own, pos_own)

    pos_flat = pos_own.reshape(-1).astype(jnp.int32)
    width = t_now.shape[1]
    step = width // NCH

    def recur(current, previous):
        outs = []
        for c in range(NCH):
            outs.append(own_rows(h_own, pos_flat, current[c], previous[c], lidx))
        return outs

    now_chunks = [t_now[:, c * step:(c + 1) * step] for c in range(NCH)]
    prev_chunks = [t_prev[:, c * step:(c + 1) * step] for c in range(NCH)]
    next_chunks = recur(now_chunks, prev_chunks)
    after_chunks = recur(next_chunks, now_chunks)
    return (jnp.concatenate(next_chunks, axis=1), jnp.concatenate(after_chunks, axis=1))


def solution(mesh):
    in_specs = (
        P("grid", "layer", None, None),
        P("grid", "layer"),
        P(("grid", "layer"), None),
        P(("grid", "layer"), None),
    )
    out_specs = (P(("grid", "layer"), None), P(("grid", "layer"), None))
    return jax.shard_map(shards, mesh=mesh, in_specs=in_specs, out_specs=out_specs, check_vma=False)
```

```python
import jax
import jax.numpy as jnp
from jax import lax
from jax.sharding import PartitionSpec as P
from jax.experimental import pallas as pl
from jax.experimental.pallas import tpu as pltpu

KB = 8
HB = 2
NCH = 2
TILE = 768


def shift(size, k):
    return [(i, (i + k) % size) for i in range(size)]


def exchange(own, lidx, block_size):
    nl = lax.axis_size("layer")
    ng = lax.axis_size("grid")
    half = own.shape[0] // 2
    from_prev = lax.ppermute(own, "layer", shift(nl, 1))
    from_next = lax.ppermute(own, "layer", shift(nl, nl - 1))
    far_a = lax.ppermute(from_prev[:half], "layer", shift(nl, 1))
    far_b = lax.ppermute(from_next[half:], "layer", shift(nl, nl - 1))
    panel = jnp.concatenate([own, from_next, far_a, far_b, from_prev], axis=0)
    rows = own.shape[0]
    width = HB * block_size
    last_at = ((nl - 1 - lidx) % nl) * rows + rows - width
    first_at = ((0 - lidx) % nl) * rows
    last = lax.dynamic_slice_in_dim(panel, last_at, width, axis=0)
    first = lax.dynamic_slice_in_dim(panel, first_at, width, axis=0)
    lo = lax.ppermute(last, "grid", shift(ng, 1))
    hi = lax.ppermute(first, "grid", shift(ng, ng - 1))
    return jnp.concatenate([panel, lo, hi], axis=0)


def step_kernel(pos_ref, h_ref, panel_ref, prev_ref, out_ref):
    rows, slots, block_size = h_ref.shape[0], h_ref.shape[1], h_ref.shape[2]
    for i in range(rows):
        acc = jnp.dot(h_ref[i, 0], panel_ref[pos_ref[i * slots]], preferred_element_type=jnp.float32)
        for s in range(1, slots):
            acc = acc + jnp.dot(h_ref[i, s], panel_ref[pos_ref[i * slots + s]], preferred_element_type=jnp.float32)
        at = slice(i * block_size, (i + 1) * block_size)
        out_ref[at, :] = (2.0 * acc - prev_ref[at, :].astype(jnp.float32)).astype(out_ref.dtype)


def own_rows(h_own, pos_flat, chunk, previous, lidx):
    block_size = h_own.shape[2]
    width = chunk.shape[1]
    tile = TILE if width % TILE == 0 else width
    wide = exchange(chunk, lidx, block_size)
    blocks = wide.reshape(wide.shape[0] // block_size, block_size, width)
    grid_spec = pltpu.PrefetchScalarGridSpec(
        num_scalar_prefetch=1,
        grid=(width // tile,),
        in_specs=[
            pl.BlockSpec(h_own.shape, lambda j, p: (0, 0, 0, 0)),
            pl.BlockSpec((blocks.shape[0], block_size, tile), lambda j, p: (0, 0, j)),
            pl.BlockSpec((chunk.shape[0], tile), lambda j, p: (0, j)),
        ],
        out_specs=pl.BlockSpec((chunk.shape[0], tile), lambda j, p: (0, j)),
    )
    return pl.pallas_call(
        step_kernel,
        grid_spec=grid_spec,
        out_shape=jax.ShapeDtypeStruct(chunk.shape, jnp.bfloat16),
        compiler_params=pltpu.CompilerParams(vmem_limit_bytes=48 * 1024 * 1024),
    )(pos_flat, h_own, blocks, previous)


def shards(h_blocks, block_cols, t_now, t_prev):
    group_rows, block_size = h_blocks.shape[0], h_blocks.shape[2]
    nl = lax.axis_size("layer")
    total_blocks = group_rows * lax.axis_size("grid")
    per_dev = group_rows // nl
    lidx = lax.axis_index("layer")
    first_block = lax.axis_index("grid") * group_rows
    rel = (block_cols - first_block + HB + total_blocks) % total_blocks

    h_split = h_blocks.reshape(nl, per_dev, *h_blocks.shape[1:])
    p_split = rel.reshape(nl, per_dev, rel.shape[1])
    h_parts = [lax.dynamic_index_in_dim(h_split, lidx, 0, keepdims=False)]
    p_parts = [lax.dynamic_index_in_dim(p_split, lidx, 0, keepdims=False)]
    for k in range(1, nl):
        dest = (lidx + k) % nl
        h_parts.append(lax.ppermute(lax.dynamic_index_in_dim(h_split, dest, 0, keepdims=False), "layer", shift(nl, k)))
        p_parts.append(lax.ppermute(lax.dynamic_index_in_dim(p_split, dest, 0, keepdims=False), "layer", shift(nl, k)))
    h_own = jnp.concatenate(h_parts, axis=1)
    rel_own = jnp.concatenate(p_parts, axis=1)
    t_now, rel_own = lax.optimization_barrier((t_now, rel_own))
    inner = rel_own - HB
    owner = inner // per_dev
    pos_own = ((owner - lidx) % nl) * per_dev + inner % per_dev
    pos_own = jnp.where(rel_own < HB, nl * per_dev + rel_own, pos_own)
    pos_own = jnp.where(rel_own >= HB + group_rows, rel_own, pos_own)

    pos_flat = pos_own.reshape(-1).astype(jnp.int32)
    width = t_now.shape[1]
    step = width // NCH

    def recur(current, previous):
        outs = []
        for c in range(NCH):
            outs.append(own_rows(h_own, pos_flat, current[c], previous[c], lidx))
        return outs

    now_chunks = [t_now[:, c * step:(c + 1) * step] for c in range(NCH)]
    prev_chunks = [t_prev[:, c * step:(c + 1) * step] for c in range(NCH)]
    next_chunks = recur(now_chunks, prev_chunks)
    after_chunks = recur(next_chunks, now_chunks)
    return (jnp.concatenate(next_chunks, axis=1), jnp.concatenate(after_chunks, axis=1))


def solution(mesh):
    in_specs = (
        P("grid", "layer", None, None),
        P("grid", "layer"),
        P(("grid", "layer"), None),
        P(("grid", "layer"), None),
    )
    out_specs = (P(("grid", "layer"), None), P(("grid", "layer"), None))
    return jax.shard_map(shards, mesh=mesh, in_specs=in_specs, out_specs=out_specs, check_vma=False)
```
